512 devices in a mesh: expert: 64 (over x, z_lo, core), shard: 8 (over z_hi, y).
Axes of the slice: x: 4, y: 4, z: 16 (z_hi: 2, z_lo: 8; z = z_hi * 8 + z_lo), core: 2. Of those that a mesh axis runs over, the one named last changes fastest.
Arguments:
- tokens: bfloat16 [2560, 4096], P('expert'), may hold values from -6 to 6
- expert_ids: int32 [2560, 8], P('expert'), may hold values from 0 to 63, all different within a row; in each aligned block of 40 rows (0 to 39, 40 to 79, ...) at most 10 rows name the same one
- route_weights: float32 [2560, 8], P('expert'), may hold values from 0.05 to 0.5
- partner: int32 [64], replicated, may hold values from 0 to 63, as said below
- gate_up: bfloat16 [64, 2, 768, 4096], P('expert', None, 'shard'), may hold values from -0.09375 to 0.09375
- down_weight: bfloat16 [64, 768, 4096], P('expert', None, 'shard'), may hold values from -0.21875 to 0.21875
- down_grad: bfloat16 [64, 128, 4096], P('expert', None, 'shard'), may hold values from -6 to 6
- moment_one: float32 [64, 128, 4096], P('expert', None, 'shard'), may hold values from -6 to 6
- moment_two: float32 [64, 128, 4096], P('expert', None, 'shard'), may hold values from 0.3 to 3
Outputs:
- combined: bfloat16 [2560, 4096], P('expert', 'shard')
- trained_rows: bfloat16 [64, 128, 4096], P('expert', None, 'shard')
- first_moment: float32 [64, 128, 4096], P('expert', None, 'shard')
- second_moment: float32 [64, 128, 4096], P('expert', None, 'shard')
The draws below stay inside these ranges and needn't reach their ends.
Inputs may be any that keep to these rules, and one draw needn't show every extreme that they name: `expert_ids`: each row names 8 different experts. In each aligned block of 40 rows (the rows held by one index of expert) no expert is named by more than 10 rows, a bound that some block reaches. partner[partner[p]] = p and partner[p] != p for every p: the list splits all 64 indices into pairs.
All inputs are finite; a program needn't handle non-finite values.
Results may differ from the reference program's by a relative error of at most 0.0058.
Values may be sent and summed in bfloat16 or wider, within the bound.
No kernel may reach another device: no remote copies, remote signals or barrier semaphores. Data moves between devices by JAX's collectives and lax.ppermute only.
A program may use at most 64 MiB of HBM per device.

```python
import math
import jax
import jax.numpy as jnp
import numpy as np
from jax import lax

D = 4096
FF = 768
HOT = 128
TOP = 8
STEP = 100
TOK_E = 40
EXPERTS = 64
CAP = 10
TOKENS = 2560
N_EXPERT = 64


def draw_partner(key, part):
    order = jax.random.permutation(key, EXPERTS).astype(jnp.int32)
    paired = order.reshape(EXPERTS // 2, 2)
    swapped = jnp.stack([paired[:, 1], paired[:, 0]], axis=1).reshape(EXPERTS)
    return jnp.zeros((EXPERTS,), jnp.int32).at[order].set(swapped)


def shard_levels(own_key, dims, shards, smallest, top_value):
    loudness, own = 1.0, jax.random.fold_in(own_key, 6)
    for dim, parts in shards:
        steps = jnp.exp(jax.random.uniform(jax.random.fold_in(own, dim), (parts,), jnp.float32, smallest / len(shards), top_value / len(shards)))
        loudness = loudness * jnp.repeat(steps, dims[dim] // parts).reshape([-1 if axis == dim else 1 for axis in range(len(dims))])
    return loudness


def assign_block(stream_key, own, number, rows, amount, top, most, skew):
    ranking = jax.random.permutation(stream_key, amount)
    heavy_load, common = shares(amount, rows * top, most, skew, True), shares(amount, rows * top, most, skew, False)
    places = jnp.arange(amount)

    def named(tallies, turn):
        used = int((tallies > 0).sum())
        fixed = max(1, used // 4)
        shifted = fixed + (places - fixed + turn * (used - fixed)) % max(1, amount - fixed)
        return jnp.zeros((amount,), jnp.int32).at[ranking[jnp.where(places < fixed, places, shifted)]].set(jnp.asarray(tallies, jnp.int32))

    tallies = jnp.where(number % 4 == 0, named(heavy_load, number // 4), named(common, number - number // 4 - 1))
    mixed = jax.random.permutation(jax.random.fold_in(own, 3), amount)
    donor, receiver = mixed[0:amount // 2 * 2:2], mixed[1:amount // 2 * 2:2]
    margin = jnp.minimum(tallies[donor] - 1, most - tallies[receiver]) // 2
    margin = jnp.where((donor == ranking[0]) | (receiver == ranking[0]) | (tallies[receiver] == 0), 0, jnp.maximum(margin, 0))
    shifted = jax.random.randint(jax.random.fold_in(own, 4), (amount // 2,), 0, 1 << 20) % (margin + 1)
    tallies = tallies.at[donor].add(-shifted).at[receiver].add(shifted)
    items = jnp.searchsorted(jnp.cumsum(tallies), jnp.arange(rows * top), side="right").astype(jnp.int32)
    grid = items.reshape(top, rows).T
    grid = grid[jax.random.permutation(jax.random.fold_in(own, 1), rows)]
    turn = jax.random.randint(jax.random.fold_in(own, 2), (rows, 1), 0, top)
    return jnp.take_along_axis(grid, (jnp.arange(top)[None, :] + turn) % top, axis=1)


def shares(number_of, total, reach, skew, full):
    loads = [(1 << 20) // math.isqrt(standing ** skew) + 1 for standing in range(1, number_of + 1)]
    largest = reach if full else min(reach, max(-(-total // number_of), total * loads[0] // sum(loads)))
    least = 1 if total - largest >= number_of - 1 else 0
    given, rest = [largest] + [least] * (number_of - 1), total - largest - least * (number_of - 1)
    while rest > 0:
        movable = [i for i in range(1, number_of) if given[i] < largest] or [i for i in range(1, number_of) if given[i] < reach]
        mass, left = sum([loads[i] for i in movable]), rest
        for i in movable:
            extra = min(reach - given[i], max(1, left * loads[i] // mass), rest)
            given[i] = given[i] + extra
            rest = rest - extra
    return np.array(given)


def gaussian(key, dims, width, bound, split=(), held_as=jnp.bfloat16):
    result = width * jax.random.normal(key, dims, jnp.float32)
    if split:
        result = result * shard_levels(key, dims, split, -0.22, 0.18)
    return jnp.clip(result, -bound, bound).astype(held_as)


def setup_inputs(seed: int = 0) -> dict:
    key_list = jax.random.split(jax.random.key(seed), 10)
    tokens = gaussian(key_list[0], (TOKENS, D), 1.0, 6.0, ((0, 64),))
    expert_ids_keys = jax.random.split(jax.random.fold_in(key_list[1], 1), TOKENS // TOK_E)
    expert_ids_turns = jax.random.permutation(jax.random.fold_in(key_list[1], 3), TOKENS // TOK_E)
    expert_ids = jax.vmap(lambda own, number: assign_block(jax.random.fold_in(key_list[1], 2), own, number, TOK_E, EXPERTS, TOP, CAP, 2))(expert_ids_keys, expert_ids_turns).reshape((TOKENS, TOP))
    route_weights = jnp.clip(jnp.exp(math.log(0.5) - 2.3025851 * jax.random.uniform(key_list[2], (TOKENS, TOP), jnp.float32) ** shard_levels(key_list[2], (TOKENS, TOP), ((0, 64),), -0.2, 0.2)), 0.05, 0.5)
    partner = draw_partner(jax.random.fold_in(key_list[9], 71), 0)
    gate_up = gaussian(key_list[4], (EXPERTS, 2, FF, D), D ** -0.5, 0.09375, ((0, 64), (2, 8)))
    down_weight = gaussian(key_list[5], (EXPERTS, FF, D), FF ** -0.5, 0.21875, ((0, 64), (2, 8)))
    down_grad = gaussian(key_list[6], (EXPERTS, HOT, D), 1.0, 6.0, ((0, 64), (2, 8)))
    moment_one = gaussian(key_list[7], (EXPERTS, HOT, D), 1.0, 6.0, ((0, 64), (2, 8)), jnp.float32)
    moment_two = jnp.clip(jnp.exp(math.log(3.0) - 2.3025851 * jax.random.uniform(key_list[8], (EXPERTS, HOT, D), jnp.float32) ** shard_levels(key_list[8], (EXPERTS, HOT, D), ((0, 64), (2, 8)), -0.2, 0.2)), 0.3, 3.0)
    return {"tokens": tokens, "expert_ids": expert_ids, "route_weights": route_weights, "partner": partner, "gate_up": gate_up, "down_weight": down_weight, "down_grad": down_grad, "moment_one": moment_one, "moment_two": moment_two}


learn_rate = 0.01
beta_one = 0.9
beta_two = 0.999
epsilon = 1e-08
decay_rate = 0.1

def adamw(weight, gradient, first, second):
    grad_wide = gradient.astype(jnp.float32)
    first_new = beta_one * first + (1.0 - beta_one) * grad_wide
    second_new = beta_two * second + (1.0 - beta_two) * grad_wide * grad_wide
    first_hat = first_new / (1.0 - beta_one ** STEP)
    second_hat = second_new / (1.0 - beta_two ** STEP)
    weight_wide = weight.astype(jnp.float32)
    updated = weight_wide - learn_rate * (first_hat / (jnp.sqrt(second_hat) + epsilon) + decay_rate * weight_wide)
    return (updated.astype(jnp.bfloat16), first_new, second_new)

def expert_rows(token_rows, gate_one, down_one):
    hidden_count = gate_one.shape[1]
    joined = gate_one.reshape(2 * hidden_count, gate_one.shape[2])
    projected = jnp.dot(token_rows, joined.T, preferred_element_type=jnp.float32)
    hidden = (jax.nn.silu(projected[:, :hidden_count]) * projected[:, hidden_count:]).astype(jnp.bfloat16)
    return jnp.dot(hidden, down_one, preferred_element_type=jnp.float32).astype(jnp.bfloat16)

def reference(tokens, expert_ids, route_weights, partner, gate_up, down_weight, down_grad, moment_one, moment_two):
    new_rows, first_new, second_new = adamw(down_weight[:, :HOT], down_grad, moment_one, moment_two)
    down_full = jnp.concatenate([new_rows, down_weight[:, HOT:]], axis=1)
    per_expert = N_EXPERT * CAP
    blocks = TOKENS // TOK_E
    assigned = expert_ids.reshape(blocks, TOK_E * TOP).astype(jnp.int32)
    experts = jnp.arange(EXPERTS, dtype=jnp.int32)
    picked = (assigned[:, :, None] == experts[None, None, :]).astype(jnp.int32)
    running = jnp.cumsum(picked, axis=1)
    rank_in_block = lax.optimization_barrier(jnp.sum((running - 1) * picked, axis=2))
    block_index = jnp.arange(blocks, dtype=jnp.int32)[:, None]
    slot_keys = (assigned * per_expert + block_index * CAP + rank_in_block).reshape(-1).astype(jnp.int32)
    token_index = jnp.repeat(jnp.arange(TOKENS, dtype=jnp.int32), TOP)
    slot_tokens = jnp.full((EXPERTS * per_expert,), TOKENS, jnp.int32).at[slot_keys].set(token_index).reshape(EXPERTS, per_expert)
    slot_weights = jnp.zeros((EXPERTS * per_expert,), jnp.float32).at[slot_keys].set(route_weights.reshape(-1).astype(jnp.float32)).reshape(EXPERTS, per_expert)
    padded = jnp.concatenate([tokens, jnp.zeros((1, D), jnp.bfloat16)], axis=0)

    def one_expert(summed, inputs):
        token_slots, weight_slots, gate_one, down_one = inputs
        outputs = expert_rows(padded[token_slots], gate_one, down_one)
        return (summed.at[token_slots].add(weight_slots[:, None] * outputs.astype(jnp.float32)), None)
    summed, unused = lax.scan(one_expert, jnp.zeros((TOKENS + 1, D), jnp.float32), (slot_tokens, slot_weights, gate_up, down_full))
    combined = summed[:TOKENS].astype(jnp.bfloat16)
    return (combined, new_rows[partner], first_new[partner], second_new[partner])
```

```python
import jax
import jax.numpy as jnp
from jax import lax
from jax.sharding import Mesh, PartitionSpec as P

STEP = 100


learn_rate = 0.01
beta_one = 0.9
beta_two = 0.999
epsilon = 1e-08
decay_rate = 0.1


def adamw(weight, gradient, first, second):
    grad_wide = gradient.astype(jnp.float32)
    first_new = beta_one * first + (1.0 - beta_one) * grad_wide
    second_new = beta_two * second + (1.0 - beta_two) * grad_wide * grad_wide
    first_hat = first_new / (1.0 - beta_one**STEP)
    second_hat = second_new / (1.0 - beta_two**STEP)
    weight_wide = weight.astype(jnp.float32)
    updated = weight_wide - learn_rate * (
        first_hat / (jnp.sqrt(second_hat) + epsilon) + decay_rate * weight_wide
    )
    return (updated.astype(jnp.bfloat16), first_new, second_new)


def relocate(rows, first, second, partner, groups):
    parts = (
        rows.reshape(groups, -1),
        first.astype(jnp.bfloat16).reshape(groups, -1),
        second.astype(jnp.bfloat16).reshape(groups, -1),
    )
    widths = [p.shape[1] for p in parts]
    payload = jnp.concatenate(parts, axis=1)
    spread = lax.all_to_all(payload, "expert", split_axis=0, concat_axis=0, tiled=True)
    back = lax.all_to_all(
        jnp.take(spread, partner, axis=0), "expert", split_axis=0, concat_axis=0, tiled=True
    )
    rows_out = back[:, : widths[0]].reshape(rows.shape)
    first_out = back[:, widths[0] : widths[0] + widths[1]].astype(jnp.float32).reshape(first.shape)
    second_out = back[:, widths[0] + widths[1] :].astype(jnp.float32).reshape(second.shape)
    return rows_out, first_out, second_out


def shards(
    tokens,
    expert_ids,
    route_weights,
    partner,
    gate_up,
    down_weight,
    down_grad,
    moment_one,
    moment_two,
):
    groups = lax.axis_size("expert")
    quarters = lax.axis_size("y")
    token_count = tokens.shape[0]
    model_width = tokens.shape[1]
    part_width = down_weight.shape[2]
    trained = down_grad.shape[1]
    capacity = 2 * token_count * expert_ids.shape[1] // groups
    quarter = model_width // quarters
    new_rows, first_new, second_new = adamw(
        down_weight[:, :trained], down_grad, moment_one, moment_two
    )
    down_new = jnp.concatenate([new_rows, down_weight[:, trained:]], axis=1)
    rows_out, first_out, second_out = relocate(new_rows, first_new, second_new, partner, groups)
    experts = jnp.arange(groups, dtype=jnp.int32)
    picked = (expert_ids[:, :, None] == experts[None, None, :]).astype(jnp.int32)
    running = jnp.cumsum(picked.reshape(-1, groups), axis=0).reshape(picked.shape)
    slot_index = jnp.sum((running - 1) * picked, axis=2)
    position = expert_ids * capacity + slot_index
    positions = jnp.arange(groups * capacity, dtype=jnp.int32)
    matches = position[None, :, :] == positions[:, None, None]
    dispatch = jnp.sum(matches.astype(jnp.int32), axis=2).astype(jnp.bfloat16)
    weighting = jnp.sum(jnp.where(matches, route_weights[None, :, :], 0.0), axis=2)
    own_quarter = lax.dynamic_slice_in_dim(tokens, lax.axis_index("y") * quarter, quarter, axis=1)
    outgoing = jnp.dot(dispatch, own_quarter, preferred_element_type=jnp.float32).astype(jnp.bfloat16)
    outgoing = outgoing.reshape(groups, capacity, quarter)
    received = lax.all_to_all(outgoing, "expert", split_axis=0, concat_axis=0, tiled=True)
    gathered = lax.all_gather(received, "y", axis=0, tiled=False)
    token_rows = gathered.reshape(quarters, groups * capacity, quarter)
    joined = gate_up.reshape(-1, quarters, quarter)
    hidden_count = joined.shape[0] // 2
    down_rows = down_new.reshape(-1, part_width)
    projected = lax.dot_general(
        token_rows, joined, (((0, 2), (1, 2)), ((), ())), preferred_element_type=jnp.float32
    )
    hidden = (jax.nn.silu(projected[:, :hidden_count]) * projected[:, hidden_count:]).astype(
        jnp.bfloat16
    )
    summed = jnp.dot(
        lax.all_gather(hidden, ("zh", "y"), axis=1, tiled=True),
        down_rows,
        preferred_element_type=jnp.float32,
    )
    results = summed.astype(jnp.bfloat16).reshape(groups, capacity, part_width)
    returned = lax.all_to_all(results, "expert", split_axis=0, concat_axis=0, tiled=True)
    returned_wide = returned.reshape(-1, part_width).astype(jnp.float32)
    combined = jnp.dot(
        weighting.T,
        returned_wide,
        precision=lax.Precision.HIGHEST,
        preferred_element_type=jnp.float32,
    ).astype(jnp.bfloat16)
    return (combined, rows_out, first_out, second_out)


def solution(mesh):
    shard_size = mesh.shape["shard"]
    quarters = 4 if shard_size % 4 == 0 else shard_size
    devices = mesh.devices.reshape(mesh.shape["expert"], shard_size // quarters, quarters)
    split_mesh = Mesh(devices, ("expert", "zh", "y"))
    sh = ("zh", "y")
    return jax.shard_map(
        shards,
        mesh=split_mesh,
        in_specs=(
            P("expert", None),
            P("expert", None),
            P("expert", None),
            P(),
            P("expert", None, sh, None),
            P("expert", None, sh),
            P("expert", None, sh),
            P("expert", None, sh),
            P("expert", None, sh),
        ),
        out_specs=(
            P("expert", sh),
            P("expert", None, sh),
            P("expert", None, sh),
            P("expert", None, sh),
        ),
        check_vma=False,
    )
```

```python
import jax
import jax.numpy as jnp
from jax import lax
from jax.sharding import Mesh, PartitionSpec as P

STEP = 100


learn_rate = 0.01
beta_one = 0.9
beta_two = 0.999
epsilon = 1e-08
decay_rate = 0.1


def adamw(weight, gradient, first, second):
    grad_wide = gradient.astype(jnp.float32)
    first_new = beta_one * first + (1.0 - beta_one) * grad_wide
    second_new = beta_two * second + (1.0 - beta_two) * grad_wide * grad_wide
    first_hat = first_new / (1.0 - beta_one**STEP)
    second_hat = second_new / (1.0 - beta_two**STEP)
    weight_wide = weight.astype(jnp.float32)
    updated = weight_wide - learn_rate * (
        first_hat / (jnp.sqrt(second_hat) + epsilon) + decay_rate * weight_wide
    )
    return (updated.astype(jnp.bfloat16), first_new, second_new)


def relocate(rows, first, second, partner, groups):
    parts = (
        rows.reshape(groups, -1),
        first.astype(jnp.bfloat16).reshape(groups, -1),
        second.astype(jnp.bfloat16).reshape(groups, -1),
    )
    widths = [p.shape[1] for p in parts]
    payload = jnp.concatenate(parts, axis=1)
    spread = lax.all_to_all(payload, "expert", split_axis=0, concat_axis=0, tiled=True)
    back = lax.all_to_all(
        jnp.take(spread, partner, axis=0), "expert", split_axis=0, concat_axis=0, tiled=True
    )
    rows_out = back[:, : widths[0]].reshape(rows.shape)
    first_out = back[:, widths[0] : widths[0] + widths[1]].astype(jnp.float32).reshape(first.shape)
    second_out = back[:, widths[0] + widths[1] :].astype(jnp.float32).reshape(second.shape)
    return rows_out, first_out, second_out


def shards(
    tokens,
    expert_ids,
    route_weights,
    partner,
    gate_up,
    down_weight,
    down_grad,
    moment_one,
    moment_two,
):
    groups = lax.axis_size("expert")
    quarters = lax.axis_size("y")
    token_count = tokens.shape[0]
    model_width = tokens.shape[1]
    part_width = down_weight.shape[2]
    trained = down_grad.shape[1]
    capacity = 2 * token_count * expert_ids.shape[1] // groups
    quarter = model_width // quarters
    new_rows, first_new, second_new = adamw(
        down_weight[:, :trained], down_grad, moment_one, moment_two
    )
    down_new = jnp.concatenate([new_rows, down_weight[:, trained:]], axis=1)
    rows_out, first_out, second_out = relocate(new_rows, first_new, second_new, partner, groups)
    experts = jnp.arange(groups, dtype=jnp.int32)
    picked = (expert_ids[:, :, None] == experts[None, None, :]).astype(jnp.int32)
    running = jnp.cumsum(picked.reshape(-1, groups), axis=0).reshape(picked.shape)
    slot_index = jnp.sum((running - 1) * picked, axis=2)
    position = expert_ids * capacity + slot_index
    positions = jnp.arange(groups * capacity, dtype=jnp.int32)
    matches = position[None, :, :] == positions[:, None, None]
    dispatch = jnp.sum(matches.astype(jnp.int32), axis=2).astype(jnp.bfloat16)
    weighting = jnp.sum(jnp.where(matches, route_weights[None, :, :], 0.0), axis=2)
    own_quarter = lax.dynamic_slice_in_dim(tokens, lax.axis_index("y") * quarter, quarter, axis=1)
    outgoing = jnp.dot(dispatch, own_quarter, preferred_element_type=jnp.float32).astype(jnp.bfloat16)
    outgoing = outgoing.reshape(groups, capacity * quarter)
    received = lax.all_to_all(outgoing, "expert", split_axis=0, concat_axis=0, tiled=True)
    received = received.reshape(groups * capacity, quarter)
    token_rows = lax.all_gather(received, "y", axis=0, tiled=False)
    joined = gate_up.reshape(-1, model_width)
    hidden_count = joined.shape[0] // 2
    projected = sum(
        lax.dot_general(
            joined[:, q * quarter : (q + 1) * quarter],
            token_rows[q],
            (((1,), (1,)), ((), ())),
            preferred_element_type=jnp.float32,
        )
        for q in range(quarters)
    )
    hidden = (jax.nn.silu(projected[:hidden_count]) * projected[hidden_count:]).astype(jnp.bfloat16)
    every_hidden = lax.all_gather(hidden, ("zh", "y"), axis=0, tiled=True)
    down_rows = down_new.reshape(-1, part_width)
    summed = lax.dot_general(
        every_hidden, down_rows, (((0,), (0,)), ((), ())), preferred_element_type=jnp.float32
    )
    results = summed.astype(jnp.bfloat16).reshape(groups, capacity * part_width)
    returned = lax.all_to_all(results, "expert", split_axis=0, concat_axis=0, tiled=True)
    returned_wide = returned.reshape(-1, part_width).astype(jnp.float32)
    combined = jnp.dot(
        weighting.T,
        returned_wide,
        precision=lax.Precision.HIGHEST,
        preferred_element_type=jnp.float32,
    ).astype(jnp.bfloat16)
    return (combined, rows_out, first_out, second_out)


def solution(mesh):
    shard_size = mesh.shape["shard"]
    quarters = 4 if shard_size % 4 == 0 else shard_size
    devices = mesh.devices.reshape(mesh.shape["expert"], shard_size // quarters, quarters)
    split_mesh = Mesh(devices, ("expert", "zh", "y"))
    sh = ("zh", "y")
    return jax.shard_map(
        shards,
        mesh=split_mesh,
        in_specs=(
            P("expert", None),
            P("expert", None),
            P("expert", None),
            P(),
            P("expert", None, sh, None),
            P("expert", None, sh),
            P("expert", None, sh),
            P("expert", None, sh),
            P("expert", None, sh),
        ),
        out_specs=(
            P("expert", sh),
            P("expert", None, sh),
            P("expert", None, sh),
            P("expert", None, sh),
        ),
        check_vma=False,
    )
```

```python
import jax
import jax.numpy as jnp
from jax import lax
from jax.sharding import Mesh, PartitionSpec as P

STEP = 100


learn_rate = 0.01
beta_one = 0.9
beta_two = 0.999
epsilon = 1e-08
decay_rate = 0.1


def adamw(weight, gradient, first, second):
    grad_wide = gradient.astype(jnp.float32)
    first_new = beta_one * first + (1.0 - beta_one) * grad_wide
    second_new = beta_two * second + (1.0 - beta_two) * grad_wide * grad_wide
    first_hat = first_new / (1.0 - beta_one**STEP)
    second_hat = second_new / (1.0 - beta_two**STEP)
    weight_wide = weight.astype(jnp.float32)
    updated = weight_wide - learn_rate * (
        first_hat / (jnp.sqrt(second_hat) + epsilon) + decay_rate * weight_wide
    )
    return (updated.astype(jnp.bfloat16), first_new, second_new)


def relocate(rows, first, second, partner, groups):
    parts = (
        rows.reshape(groups, -1),
        first.astype(jnp.bfloat16).reshape(groups, -1),
        second.astype(jnp.bfloat16).reshape(groups, -1),
    )
    widths = [p.shape[1] for p in parts]
    payload = jnp.concatenate(parts, axis=1)
    spread = lax.all_to_all(payload, "expert", split_axis=0, concat_axis=0, tiled=True)
    back = lax.all_to_all(
        jnp.take(spread, partner, axis=0), "expert", split_axis=0, concat_axis=0, tiled=True
    )
    rows_out = back[:, : widths[0]].reshape(rows.shape)
    first_out = back[:, widths[0] : widths[0] + widths[1]].astype(jnp.float32).reshape(first.shape)
    second_out = back[:, widths[0] + widths[1] :].astype(jnp.float32).reshape(second.shape)
    return rows_out, first_out, second_out


def shards(
    tokens,
    expert_ids,
    route_weights,
    partner,
    gate_up,
    down_weight,
    down_grad,
    moment_one,
    moment_two,
):
    groups = lax.axis_size("expert")
    quarters = lax.axis_size("y")
    token_count = tokens.shape[0]
    model_width = tokens.shape[1]
    part_width = down_weight.shape[2]
    trained = down_grad.shape[1]
    capacity = 2 * token_count * expert_ids.shape[1] // groups
    quarter = model_width // quarters
    new_rows, first_new, second_new = adamw(
        down_weight[:, :trained], down_grad, moment_one, moment_two
    )
    down_new = jnp.concatenate([new_rows, down_weight[:, trained:]], axis=1)
    rows_out, first_out, second_out = relocate(new_rows, first_new, second_new, partner, groups)
    experts = jnp.arange(groups, dtype=jnp.int32)
    picked = (expert_ids[:, :, None] == experts[None, None, :]).astype(jnp.int32)
    running = jnp.cumsum(picked.reshape(-1, groups), axis=0).reshape(picked.shape)
    slot_index = jnp.sum((running - 1) * picked, axis=2)
    position = expert_ids * capacity + slot_index
    positions = jnp.arange(groups * capacity, dtype=jnp.int32)
    matches = position[None, :, :] == positions[:, None, None]
    dispatch = jnp.sum(matches.astype(jnp.int32), axis=2).astype(jnp.bfloat16)
    weighting = jnp.sum(jnp.where(matches, route_weights[None, :, :], 0.0), axis=2)
    own_quarter = lax.dynamic_slice_in_dim(tokens, lax.axis_index("y") * quarter, quarter, axis=1)
    outgoing = jnp.dot(dispatch, own_quarter, preferred_element_type=jnp.float32).astype(jnp.bfloat16)
    outgoing = outgoing.reshape(groups, capacity * quarter)
    received = lax.all_to_all(outgoing, "expert", split_axis=0, concat_axis=0, tiled=True)
    received = received.reshape(groups * capacity, quarter)
    token_rows = lax.all_gather(received, "y", axis=0, tiled=False)
    joined = gate_up.reshape(-1, model_width)
    hidden_count = joined.shape[0] // 2
    projected = sum(
        lax.dot_general(
            joined[:, q * quarter : (q + 1) * quarter],
            token_rows[q],
            (((1,), (1,)), ((), ())),
            preferred_element_type=jnp.float32,
        )
        for q in range(quarters)
    )
    hidden = (jax.nn.silu(projected[:hidden_count]) * projected[hidden_count:]).astype(jnp.bfloat16)
    shard_count = lax.axis_size(("zh", "y"))
    copies = jnp.broadcast_to(hidden.reshape(1, -1), (shard_count, hidden.size))
    every_hidden = lax.all_to_all(copies, ("zh", "y"), split_axis=0, concat_axis=0, tiled=True)
    every_hidden = every_hidden.reshape(shard_count * hidden_count, -1)
    down_rows = down_new.reshape(-1, part_width)
    summed = lax.dot_general(
        every_hidden, down_rows, (((0,), (0,)), ((), ())), preferred_element_type=jnp.float32
    )
    results = summed.astype(jnp.bfloat16).reshape(groups, capacity * part_width)
    returned = lax.all_to_all(results, "expert", split_axis=0, concat_axis=0, tiled=True)
    returned_wide = returned.reshape(-1, part_width).astype(jnp.float32)
    combined = jnp.dot(
        weighting.T,
        returned_wide,
        precision=lax.Precision.HIGHEST,
        preferred_element_type=jnp.float32,
    ).astype(jnp.bfloat16)
    return (combined, rows_out, first_out, second_out)


def solution(mesh):
    shard_size = mesh.shape["shard"]
    quarters = 4 if shard_size % 4 == 0 else shard_size
    devices = mesh.devices.reshape(mesh.shape["expert"], shard_size // quarters, quarters)
    split_mesh = Mesh(devices, ("expert", "zh", "y"))
    sh = ("zh", "y")
    return jax.shard_map(
        shards,
        mesh=split_mesh,
        in_specs=(
            P("expert", None),
            P("expert", None),
            P("expert", None),
            P(),
            P("expert", None, sh, None),
            P("expert", None, sh),
            P("expert", None, sh),
            P("expert", None, sh),
            P("expert", None, sh),
        ),
        out_specs=(
            P("expert", sh),
            P("expert", None, sh),
            P("expert", None, sh),
            P("expert", None, sh),
        ),
        check_vma=False,
    )
```

```python
import jax
import jax.numpy as jnp
from jax import lax
from jax.sharding import Mesh, PartitionSpec as P

STEP = 100


learn_rate = 0.01
beta_one = 0.9
beta_two = 0.999
epsilon = 1e-08
decay_rate = 0.1


def adamw(weight, gradient, first, second):
    grad_wide = gradient.astype(jnp.float32)
    first_new = beta_one * first + (1.0 - beta_one) * grad_wide
    second_new = beta_two * second + (1.0 - beta_two) * grad_wide * grad_wide
    first_hat = first_new / (1.0 - beta_one**STEP)
    second_hat = second_new / (1.0 - beta_two**STEP)
    weight_wide = weight.astype(jnp.float32)
    updated = weight_wide - learn_rate * (
        first_hat / (jnp.sqrt(second_hat) + epsilon) + decay_rate * weight_wide
    )
    return (updated.astype(jnp.bfloat16), first_new, second_new)


def shards(
    tokens,
    expert_ids,
    route_weights,
    partner,
    gate_up,
    down_weight,
    down_grad,
    moment_one,
    moment_two,
):
    groups = lax.axis_size("expert")
    quarters = lax.axis_size("y")
    token_count = tokens.shape[0]
    model_width = tokens.shape[1]
    part_width = down_weight.shape[2]
    trained = down_grad.shape[1]
    capacity = 2 * token_count * expert_ids.shape[1] // groups
    quarter = model_width // quarters
    new_rows, first_new, second_new = adamw(
        down_weight[:, :trained], down_grad, moment_one, moment_two
    )
    down_new = jnp.concatenate([new_rows, down_weight[:, trained:]], axis=1)
    pieces = (
        new_rows.reshape(groups, -1),
        first_new.astype(jnp.bfloat16).reshape(groups, -1),
        second_new.astype(jnp.bfloat16).reshape(groups, -1),
    )
    piece_width = sum(p.shape[1] for p in pieces)
    experts = jnp.arange(groups, dtype=jnp.int32)
    picked = (expert_ids[:, :, None] == experts[None, None, :]).astype(jnp.int32)
    running = jnp.cumsum(picked.reshape(-1, groups), axis=0).reshape(picked.shape)
    slot_index = jnp.sum((running - 1) * picked, axis=2)
    position = expert_ids * capacity + slot_index
    positions = jnp.arange(groups * capacity, dtype=jnp.int32)
    matches = position[None, :, :] == positions[:, None, None]
    dispatch = jnp.sum(matches.astype(jnp.int32), axis=2).astype(jnp.bfloat16)
    weighting = jnp.sum(jnp.where(matches, route_weights[None, :, :], 0.0), axis=2)
    own_quarter = lax.dynamic_slice_in_dim(tokens, lax.axis_index("y") * quarter, quarter, axis=1)
    outgoing = jnp.dot(dispatch, own_quarter, preferred_element_type=jnp.float32).astype(jnp.bfloat16)
    outgoing = jnp.concatenate([outgoing.reshape(groups, capacity * quarter)] + list(pieces), axis=1)
    received = lax.all_to_all(outgoing, "expert", split_axis=0, concat_axis=0, tiled=True)
    spread = received[:, capacity * quarter :]
    received = received[:, : capacity * quarter].reshape(groups * capacity, quarter)
    token_rows = lax.all_gather(received, "y", axis=0, tiled=False)
    joined = gate_up.reshape(-1, model_width)
    hidden_count = joined.shape[0] // 2
    projected = sum(
        lax.dot_general(
            joined[:, q * quarter : (q + 1) * quarter],
            token_rows[q],
            (((1,), (1,)), ((), ())),
            preferred_element_type=jnp.float32,
        )
        for q in range(quarters)
    )
    hidden = (jax.nn.silu(projected[:hidden_count]) * projected[hidden_count:]).astype(jnp.bfloat16)
    shard_count = lax.axis_size(("zh", "y"))
    copies = jnp.broadcast_to(hidden.reshape(1, -1), (shard_count, hidden.size))
    every_hidden = lax.all_to_all(copies, ("zh", "y"), split_axis=0, concat_axis=0, tiled=True)
    every_hidden = every_hidden.reshape(shard_count * hidden_count, -1)
    down_rows = down_new.reshape(-1, part_width)
    summed = lax.dot_general(
        every_hidden, down_rows, (((0,), (0,)), ((), ())), preferred_element_type=jnp.float32
    )
    results = summed.astype(jnp.bfloat16).reshape(groups, capacity * part_width)
    results = jnp.concatenate([results, jnp.take(spread, partner, axis=0)], axis=1)
    returned = lax.all_to_all(results, "expert", split_axis=0, concat_axis=0, tiled=True)
    back = returned[:, capacity * part_width :]
    returned = returned[:, : capacity * part_width]
    widths = [p.shape[1] for p in pieces]
    rows_out = back[:, : widths[0]].reshape(new_rows.shape)
    first_out = back[:, widths[0] : widths[0] + widths[1]].astype(jnp.float32).reshape(first_new.shape)
    second_out = back[:, widths[0] + widths[1] :].astype(jnp.float32).reshape(second_new.shape)
    returned_wide = returned.reshape(-1, part_width).astype(jnp.float32)
    combined = jnp.dot(
        weighting.T,
        returned_wide,
        precision=lax.Precision.HIGHEST,
        preferred_element_type=jnp.float32,
    ).astype(jnp.bfloat16)
    return (combined, rows_out, first_out, second_out)


def solution(mesh):
    shard_size = mesh.shape["shard"]
    quarters = 4 if shard_size % 4 == 0 else shard_size
    devices = mesh.devices.reshape(mesh.shape["expert"], shard_size // quarters, quarters)
    split_mesh = Mesh(devices, ("expert", "zh", "y"))
    sh = ("zh", "y")
    return jax.shard_map(
        shards,
        mesh=split_mesh,
        in_specs=(
            P("expert", None),
            P("expert", None),
            P("expert", None),
            P(),
            P("expert", None, sh, None),
            P("expert", None, sh),
            P("expert", None, sh),
            P("expert", None, sh),
            P("expert", None, sh),
        ),
        out_specs=(
            P("expert", sh),
            P("expert", None, sh),
            P("expert", None, sh),
            P("expert", None, sh),
        ),
        check_vma=False,
    )
```

```python
import jax
import jax.numpy as jnp
from jax import lax
from jax.sharding import Mesh, PartitionSpec as P

STEP = 100


learn_rate = 0.01
beta_one = 0.9
beta_two = 0.999
epsilon = 1e-08
decay_rate = 0.1


def adamw(weight, gradient, first, second):
    grad_wide = gradient.astype(jnp.float32)
    first_new = beta_one * first + (1.0 - beta_one) * grad_wide
    second_new = beta_two * second + (1.0 - beta_two) * grad_wide * grad_wide
    first_hat = first_new / (1.0 - beta_one**STEP)
    second_hat = second_new / (1.0 - beta_two**STEP)
    weight_wide = weight.astype(jnp.float32)
    updated = weight_wide - learn_rate * (
        first_hat / (jnp.sqrt(second_hat) + epsilon) + decay_rate * weight_wide
    )
    return (updated.astype(jnp.bfloat16), first_new, second_new)


def shards(
    tokens,
    expert_ids,
    route_weights,
    partner,
    gate_up,
    down_weight,
    down_grad,
    moment_one,
    moment_two,
):
    groups = lax.axis_size("expert")
    quarters = lax.axis_size("y")
    token_count = tokens.shape[0]
    model_width = tokens.shape[1]
    part_width = down_weight.shape[2]
    trained = down_grad.shape[1]
    capacity = 2 * token_count * expert_ids.shape[1] // groups
    quarter = model_width // quarters
    new_rows, first_new, second_new = adamw(
        down_weight[:, :trained], down_grad, moment_one, moment_two
    )
    down_new = jnp.concatenate([new_rows, down_weight[:, trained:]], axis=1)
    pieces = (
        new_rows.reshape(groups, -1),
        first_new.astype(jnp.bfloat16).reshape(groups, -1),
        second_new.astype(jnp.bfloat16).reshape(groups, -1),
    )
    piece_width = sum(p.shape[1] for p in pieces)
    experts = jnp.arange(groups, dtype=jnp.int32)
    picked = (expert_ids[:, :, None] == experts[None, None, :]).astype(jnp.int32)
    running = jnp.cumsum(picked.reshape(-1, groups), axis=0).reshape(picked.shape)
    slot_index = jnp.sum((running - 1) * picked, axis=2)
    position = expert_ids * capacity + slot_index
    positions = jnp.arange(groups * capacity, dtype=jnp.int32)
    matches = position[None, :, :] == positions[:, None, None]
    dispatch = jnp.sum(matches.astype(jnp.int32), axis=2).astype(jnp.bfloat16)
    weighting = jnp.sum(jnp.where(matches, route_weights[None, :, :], 0.0), axis=2)
    own_quarter = lax.dynamic_slice_in_dim(tokens, lax.axis_index("y") * quarter, quarter, axis=1)
    outgoing = jnp.dot(dispatch, own_quarter, preferred_element_type=jnp.float32).astype(jnp.bfloat16)
    outgoing = jnp.concatenate([outgoing.reshape(groups, capacity * quarter)] + list(pieces), axis=1)
    joined = gate_up.reshape(-1, quarters, quarter)
    hidden_count = joined.shape[0] // 2
    by_quarter = jnp.moveaxis(joined, 1, 0)
    quarter_weights = lax.all_to_all(by_quarter, "y", split_axis=0, concat_axis=0, tiled=True)
    quarter_weights, outgoing = lax.optimization_barrier((quarter_weights, outgoing))
    received = lax.all_to_all(outgoing, "expert", split_axis=0, concat_axis=0, tiled=True)
    spread = received[:, capacity * quarter :]
    received = received[:, : capacity * quarter].reshape(groups * capacity, quarter)
    partial = lax.dot_general(
        quarter_weights, received, (((2,), (1,)), ((), ())), preferred_element_type=jnp.float32
    )
    projected = lax.psum_scatter(partial, "y", scatter_dimension=0, tiled=False)
    hidden = (jax.nn.silu(projected[:hidden_count]) * projected[hidden_count:]).astype(jnp.bfloat16)
    shard_count = lax.axis_size(("zh", "y"))
    copies = jnp.broadcast_to(hidden.reshape(1, -1), (shard_count, hidden.size))
    every_hidden = lax.all_to_all(copies, ("zh", "y"), split_axis=0, concat_axis=0, tiled=True)
    every_hidden = every_hidden.reshape(shard_count * hidden_count, -1)
    down_rows = down_new.reshape(-1, part_width)
    summed = lax.dot_general(
        every_hidden, down_rows, (((0,), (0,)), ((), ())), preferred_element_type=jnp.float32
    )
    results = summed.astype(jnp.bfloat16).reshape(groups, capacity * part_width)
    results = jnp.concatenate([results, jnp.take(spread, partner, axis=0)], axis=1)
    returned = lax.all_to_all(results, "expert", split_axis=0, concat_axis=0, tiled=True)
    back = returned[:, capacity * part_width :]
    returned = returned[:, : capacity * part_width]
    widths = [p.shape[1] for p in pieces]
    rows_out = back[:, : widths[0]].reshape(new_rows.shape)
    first_out = back[:, widths[0] : widths[0] + widths[1]].astype(jnp.float32).reshape(first_new.shape)
    second_out = back[:, widths[0] + widths[1] :].astype(jnp.float32).reshape(second_new.shape)
    returned_wide = returned.reshape(-1, part_width).astype(jnp.float32)
    combined = jnp.dot(
        weighting.T,
        returned_wide,
        precision=lax.Precision.HIGHEST,
        preferred_element_type=jnp.float32,
    ).astype(jnp.bfloat16)
    return (combined, rows_out, first_out, second_out)


def solution(mesh):
    shard_size = mesh.shape["shard"]
    quarters = 4 if shard_size % 4 == 0 else shard_size
    devices = mesh.devices.reshape(mesh.shape["expert"], shard_size // quarters, quarters)
    split_mesh = Mesh(devices, ("expert", "zh", "y"))
    sh = ("zh", "y")
    return jax.shard_map(
        shards,
        mesh=split_mesh,
        in_specs=(
            P("expert", None),
            P("expert", None),
            P("expert", None),
            P(),
            P("expert", None, sh, None),
            P("expert", None, sh),
            P("expert", None, sh),
            P("expert", None, sh),
            P("expert", None, sh),
        ),
        out_specs=(
            P("expert", sh),
            P("expert", None, sh),
            P("expert", None, sh),
            P("expert", None, sh),
        ),
        check_vma=False,
    )
```

```python
import jax
import jax.numpy as jnp
from jax import lax
from jax.sharding import Mesh, PartitionSpec as P

STEP = 100


learn_rate = 0.01
beta_one = 0.9
beta_two = 0.999
epsilon = 1e-08
decay_rate = 0.1


def adamw(weight, gradient, first, second):
    grad_wide = gradient.astype(jnp.float32)
    first_new = beta_one * first + (1.0 - beta_one) * grad_wide
    second_new = beta_two * second + (1.0 - beta_two) * grad_wide * grad_wide
    first_hat = first_new / (1.0 - beta_one**STEP)
    second_hat = second_new / (1.0 - beta_two**STEP)
    weight_wide = weight.astype(jnp.float32)
    updated = weight_wide - learn_rate * (
        first_hat / (jnp.sqrt(second_hat) + epsilon) + decay_rate * weight_wide
    )
    return (updated.astype(jnp.bfloat16), first_new, second_new)


def shards(
    tokens,
    expert_ids,
    route_weights,
    partner,
    gate_up,
    down_weight,
    down_grad,
    moment_one,
    moment_two,
):
    groups = lax.axis_size("expert")
    quarters = lax.axis_size("y")
    token_count = tokens.shape[0]
    model_width = tokens.shape[1]
    part_width = down_weight.shape[2]
    trained = down_grad.shape[1]
    capacity = 2 * token_count * expert_ids.shape[1] // groups
    quarter = model_width // quarters
    new_rows, first_new, second_new = adamw(
        down_weight[:, :trained], down_grad, moment_one, moment_two
    )
    down_new = jnp.concatenate([new_rows, down_weight[:, trained:]], axis=1)
    pieces = (
        new_rows.reshape(groups, -1),
        first_new.astype(jnp.bfloat16).reshape(groups, -1),
        second_new.astype(jnp.bfloat16).reshape(groups, -1),
    )
    piece_width = sum(p.shape[1] for p in pieces)
    experts = jnp.arange(groups, dtype=jnp.int32)
    picked = (expert_ids[:, :, None] == experts[None, None, :]).astype(jnp.int32)
    running = jnp.cumsum(picked.reshape(-1, groups), axis=0).reshape(picked.shape)
    slot_index = jnp.sum((running - 1) * picked, axis=2)
    position = expert_ids * capacity + slot_index
    positions = jnp.arange(groups * capacity, dtype=jnp.int32)
    matches = position[None, :, :] == positions[:, None, None]
    dispatch = jnp.sum(matches.astype(jnp.int32), axis=2).astype(jnp.bfloat16)
    weighting = jnp.sum(jnp.where(matches, route_weights[None, :, :], 0.0), axis=2)
    own_quarter = lax.dynamic_slice_in_dim(tokens, lax.axis_index("y") * quarter, quarter, axis=1)
    outgoing = jnp.dot(dispatch, own_quarter, preferred_element_type=jnp.float32).astype(jnp.bfloat16)
    outgoing = jnp.concatenate([outgoing.reshape(groups, capacity * quarter)] + list(pieces), axis=1)
    joined = gate_up.reshape(-1, quarters, quarter)
    hidden_count = joined.shape[0] // 2
    every_weight = lax.all_gather(gate_up.reshape(-1, model_width), "y", axis=0, tiled=False)
    quarter_weights = lax.dynamic_slice_in_dim(every_weight, lax.axis_index("y") * quarter, quarter, axis=2)
    received = lax.all_to_all(outgoing, "expert", split_axis=0, concat_axis=0, tiled=True)
    spread = received[:, capacity * quarter :]
    received = received[:, : capacity * quarter].reshape(groups * capacity, quarter)
    partial = lax.dot_general(
        quarter_weights, received, (((2,), (1,)), ((), ())), preferred_element_type=jnp.float32
    )
    projected = lax.psum_scatter(partial, "y", scatter_dimension=0, tiled=False)
    hidden = (jax.nn.silu(projected[:hidden_count]) * projected[hidden_count:]).astype(jnp.bfloat16)
    shard_count = lax.axis_size(("zh", "y"))
    copies = jnp.broadcast_to(hidden.reshape(1, -1), (shard_count, hidden.size))
    every_hidden = lax.all_to_all(copies, ("zh", "y"), split_axis=0, concat_axis=0, tiled=True)
    every_hidden = every_hidden.reshape(shard_count * hidden_count, -1)
    down_rows = down_new.reshape(-1, part_width)
    summed = lax.dot_general(
        every_hidden, down_rows, (((0,), (0,)), ((), ())), preferred_element_type=jnp.float32
    )
    results = summed.astype(jnp.bfloat16).reshape(groups, capacity * part_width)
    results = jnp.concatenate([results, jnp.take(spread, partner, axis=0)], axis=1)
    returned = lax.all_to_all(results, "expert", split_axis=0, concat_axis=0, tiled=True)
    back = returned[:, capacity * part_width :]
    returned = returned[:, : capacity * part_width]
    widths = [p.shape[1] for p in pieces]
    rows_out = back[:, : widths[0]].reshape(new_rows.shape)
    first_out = back[:, widths[0] : widths[0] + widths[1]].astype(jnp.float32).reshape(first_new.shape)
    second_out = back[:, widths[0] + widths[1] :].astype(jnp.float32).reshape(second_new.shape)
    returned_wide = returned.reshape(-1, part_width).astype(jnp.float32)
    combined = jnp.dot(
        weighting.T,
        returned_wide,
        precision=lax.Precision.HIGHEST,
        preferred_element_type=jnp.float32,
    ).astype(jnp.bfloat16)
    return (combined, rows_out, first_out, second_out)


def solution(mesh):
    shard_size = mesh.shape["shard"]
    quarters = 4 if shard_size % 4 == 0 else shard_size
    devices = mesh.devices.reshape(mesh.shape["expert"], shard_size // quarters, quarters)
    split_mesh = Mesh(devices, ("expert", "zh", "y"))
    sh = ("zh", "y")
    return jax.shard_map(
        shards,
        mesh=split_mesh,
        in_specs=(
            P("expert", None),
            P("expert", None),
            P("expert", None),
            P(),
            P("expert", None, sh, None),
            P("expert", None, sh),
            P("expert", None, sh),
            P("expert", None, sh),
            P("expert", None, sh),
        ),
        out_specs=(
            P("expert", sh),
            P("expert", None, sh),
            P("expert", None, sh),
            P("expert", None, sh),
        ),
        check_vma=False,
    )
```

```python
import jax
import jax.numpy as jnp
from jax import lax
from jax.sharding import Mesh, PartitionSpec as P

STEP = 100


learn_rate = 0.01
beta_one = 0.9
beta_two = 0.999
epsilon = 1e-08
decay_rate = 0.1


def adamw(weight, gradient, first, second):
    grad_wide = gradient.astype(jnp.float32)
    first_new = beta_one * first + (1.0 - beta_one) * grad_wide
    second_new = beta_two * second + (1.0 - beta_two) * grad_wide * grad_wide
    first_hat = first_new / (1.0 - beta_one**STEP)
    second_hat = second_new / (1.0 - beta_two**STEP)
    weight_wide = weight.astype(jnp.float32)
    updated = weight_wide - learn_rate * (
        first_hat / (jnp.sqrt(second_hat) + epsilon) + decay_rate * weight_wide
    )
    return (updated.astype(jnp.bfloat16), first_new, second_new)


def shards(
    tokens,
    expert_ids,
    route_weights,
    partner,
    gate_up,
    down_weight,
    down_grad,
    moment_one,
    moment_two,
):
    groups = lax.axis_size("expert")
    quarters = lax.axis_size("y")
    token_count = tokens.shape[0]
    model_width = tokens.shape[1]
    part_width = down_weight.shape[2]
    trained = down_grad.shape[1]
    capacity = 2 * token_count * expert_ids.shape[1] // groups
    quarter = model_width // quarters
    new_rows, first_new, second_new = adamw(
        down_weight[:, :trained], down_grad, moment_one, moment_two
    )
    down_new = jnp.concatenate([new_rows, down_weight[:, trained:]], axis=1)
    pieces = (
        new_rows.reshape(groups, -1),
        first_new.astype(jnp.bfloat16).reshape(groups, -1),
        second_new.astype(jnp.bfloat16).reshape(groups, -1),
    )
    piece_width = sum(p.shape[1] for p in pieces)
    experts = jnp.arange(groups, dtype=jnp.int32)
    picked = (expert_ids[:, :, None] == experts[None, None, :]).astype(jnp.int32)
    running = jnp.cumsum(picked.reshape(-1, groups), axis=0).reshape(picked.shape)
    slot_index = jnp.sum((running - 1) * picked, axis=2)
    position = expert_ids * capacity + slot_index
    positions = jnp.arange(groups * capacity, dtype=jnp.int32)
    matches = position[None, :, :] == positions[:, None, None]
    dispatch = jnp.sum(matches.astype(jnp.int32), axis=2).astype(jnp.bfloat16)
    weighting = jnp.sum(jnp.where(matches, route_weights[None, :, :], 0.0), axis=2)
    own_quarter = lax.dynamic_slice_in_dim(tokens, lax.axis_index("y") * quarter, quarter, axis=1)
    outgoing = jnp.dot(dispatch, own_quarter, preferred_element_type=jnp.float32).astype(jnp.bfloat16)
    outgoing = jnp.concatenate([outgoing.reshape(groups, capacity * quarter)] + list(pieces), axis=1)
    joined = gate_up.reshape(-1, quarters, quarter)
    hidden_count = joined.shape[0] // 2
    every_weight = lax.all_gather(gate_up.reshape(-1, model_width), "y", axis=0, tiled=False)
    quarter_weights = lax.dynamic_slice_in_dim(every_weight, lax.axis_index("y") * quarter, quarter, axis=2)
    received = lax.all_to_all(outgoing, "expert", split_axis=0, concat_axis=0, tiled=True)
    spread = received[:, capacity * quarter :]
    received = received[:, : capacity * quarter].reshape(groups * capacity, quarter)
    partial = lax.dot_general(
        quarter_weights, received, (((2,), (1,)), ((), ())), preferred_element_type=jnp.float32
    )
    projected = lax.psum_scatter(partial, "y", scatter_dimension=0, tiled=False)
    hidden = (jax.nn.silu(projected[:hidden_count]) * projected[hidden_count:]).astype(jnp.bfloat16)
    back = lax.all_to_all(jnp.take(spread, partner, axis=0), "expert", split_axis=0, concat_axis=0, tiled=True)
    every_hidden = lax.all_gather(hidden, ("zh", "y"), axis=0, tiled=False)
    every_hidden = every_hidden.reshape(-1, hidden.shape[1])
    down_rows = down_new.reshape(-1, part_width)
    summed = lax.dot_general(
        every_hidden, down_rows, (((0,), (0,)), ((), ())), preferred_element_type=jnp.float32
    )
    results = summed.astype(jnp.bfloat16).reshape(groups, capacity * part_width)
    returned = lax.all_to_all(results, "expert", split_axis=0, concat_axis=0, tiled=True)
    widths = [p.shape[1] for p in pieces]
    rows_out = back[:, : widths[0]].reshape(new_rows.shape)
    first_out = back[:, widths[0] : widths[0] + widths[1]].astype(jnp.float32).reshape(first_new.shape)
    second_out = back[:, widths[0] + widths[1] :].astype(jnp.float32).reshape(second_new.shape)
    returned_wide = returned.reshape(-1, part_width).astype(jnp.float32)
    combined = jnp.dot(
        weighting.T,
        returned_wide,
        precision=lax.Precision.HIGHEST,
        preferred_element_type=jnp.float32,
    ).astype(jnp.bfloat16)
    return (combined, rows_out, first_out, second_out)


def solution(mesh):
    shard_size = mesh.shape["shard"]
    quarters = 4 if shard_size % 4 == 0 else shard_size
    devices = mesh.devices.reshape(mesh.shape["expert"], shard_size // quarters, quarters)
    split_mesh = Mesh(devices, ("expert", "zh", "y"))
    sh = ("zh", "y")
    return jax.shard_map(
        shards,
        mesh=split_mesh,
        in_specs=(
            P("expert", None),
            P("expert", None),
            P("expert", None),
            P(),
            P("expert", None, sh, None),
            P("expert", None, sh),
            P("expert", None, sh),
            P("expert", None, sh),
            P("expert", None, sh),
        ),
        out_specs=(
            P("expert", sh),
            P("expert", None, sh),
            P("expert", None, sh),
            P("expert", None, sh),
        ),
        check_vma=False,
    )
```

```python
import jax
import jax.numpy as jnp
from jax import lax
from jax.sharding import Mesh, PartitionSpec as P

STEP = 100


learn_rate = 0.01
beta_one = 0.9
beta_two = 0.999
epsilon = 1e-08
decay_rate = 0.1


def adamw(weight, gradient, first, second):
    grad_wide = gradient.astype(jnp.float32)
    first_new = beta_one * first + (1.0 - beta_one) * grad_wide
    second_new = beta_two * second + (1.0 - beta_two) * grad_wide * grad_wide
    first_hat = first_new / (1.0 - beta_one**STEP)
    second_hat = second_new / (1.0 - beta_two**STEP)
    weight_wide = weight.astype(jnp.float32)
    updated = weight_wide - learn_rate * (
        first_hat / (jnp.sqrt(second_hat) + epsilon) + decay_rate * weight_wide
    )
    return (updated.astype(jnp.bfloat16), first_new, second_new)


def shards(
    tokens,
    expert_ids,
    route_weights,
    partner,
    gate_up,
    down_weight,
    down_grad,
    moment_one,
    moment_two,
):
    groups = lax.axis_size("expert")
    quarters = lax.axis_size("y")
    token_count = tokens.shape[0]
    model_width = tokens.shape[1]
    part_width = down_weight.shape[2]
    trained = down_grad.shape[1]
    capacity = 2 * token_count * expert_ids.shape[1] // groups
    quarter = model_width // quarters
    new_rows, first_new, second_new = adamw(
        down_weight[:, :trained], down_grad, moment_one, moment_two
    )
    down_new = jnp.concatenate([new_rows, down_weight[:, trained:]], axis=1)
    pieces = (
        new_rows.reshape(groups, -1),
        first_new.astype(jnp.bfloat16).reshape(groups, -1),
        second_new.astype(jnp.bfloat16).reshape(groups, -1),
    )
    piece_width = sum(p.shape[1] for p in pieces)
    experts = jnp.arange(groups, dtype=jnp.int32)
    picked = (expert_ids[:, :, None] == experts[None, None, :]).astype(jnp.int32)
    running = jnp.cumsum(picked.reshape(-1, groups), axis=0).reshape(picked.shape)
    slot_index = jnp.sum((running - 1) * picked, axis=2)
    position = expert_ids * capacity + slot_index
    positions = jnp.arange(groups * capacity, dtype=jnp.int32)
    matches = position[None, :, :] == positions[:, None, None]
    dispatch = jnp.sum(matches.astype(jnp.int32), axis=2).astype(jnp.bfloat16)
    weighting = jnp.sum(jnp.where(matches, route_weights[None, :, :], 0.0), axis=2)
    own_quarter = lax.dynamic_slice_in_dim(tokens, lax.axis_index("y") * quarter, quarter, axis=1)
    outgoing = jnp.dot(dispatch, own_quarter, preferred_element_type=jnp.float32).astype(jnp.bfloat16)
    outgoing = jnp.concatenate([outgoing.reshape(groups, capacity * quarter)] + list(pieces), axis=1)
    joined = gate_up.reshape(-1, quarters, quarter)
    hidden_count = joined.shape[0] // 2
    every_weight = lax.all_gather(gate_up.reshape(-1, model_width), "y", axis=0, tiled=False)
    quarter_weights = lax.dynamic_slice_in_dim(every_weight, lax.axis_index("y") * quarter, quarter, axis=2)
    received = lax.all_to_all(outgoing, "expert", split_axis=0, concat_axis=0, tiled=True)
    spread = received[:, capacity * quarter :]
    received = received[:, : capacity * quarter].reshape(groups * capacity, quarter)
    partial = lax.dot_general(
        quarter_weights, received, (((2,), (1,)), ((), ())), preferred_element_type=jnp.float32
    )
    projected = lax.psum_scatter(partial, "y", scatter_dimension=0, tiled=False)
    hidden = (jax.nn.silu(projected[:hidden_count]) * projected[hidden_count:]).astype(jnp.bfloat16)
    back = lax.all_to_all(jnp.take(spread, partner, axis=0), "expert", split_axis=0, concat_axis=0, tiled=True)
    back, hidden = lax.optimization_barrier((back, hidden))
    shard_count = lax.axis_size(("zh", "y"))
    copies = jnp.broadcast_to(hidden.reshape(1, -1), (shard_count, hidden.size))
    every_hidden = lax.all_to_all(copies, ("zh", "y"), split_axis=0, concat_axis=0, tiled=True)
    every_hidden = every_hidden.reshape(shard_count * hidden_count, -1)
    down_rows = down_new.reshape(-1, part_width)
    summed = lax.dot_general(
        every_hidden, down_rows, (((0,), (0,)), ((), ())), preferred_element_type=jnp.float32
    )
    results = summed.astype(jnp.bfloat16).reshape(groups, capacity * part_width)
    returned = lax.all_to_all(results, "expert", split_axis=0, concat_axis=0, tiled=True)
    widths = [p.shape[1] for p in pieces]
    rows_out = back[:, : widths[0]].reshape(new_rows.shape)
    first_out = back[:, widths[0] : widths[0] + widths[1]].astype(jnp.float32).reshape(first_new.shape)
    second_out = back[:, widths[0] + widths[1] :].astype(jnp.float32).reshape(second_new.shape)
    returned_wide = returned.reshape(-1, part_width).astype(jnp.float32)
    combined = jnp.dot(
        weighting.T,
        returned_wide,
        precision=lax.Precision.HIGHEST,
        preferred_element_type=jnp.float32,
    ).astype(jnp.bfloat16)
    return (combined, rows_out, first_out, second_out)


def solution(mesh):
    shard_size = mesh.shape["shard"]
    quarters = 4 if shard_size % 4 == 0 else shard_size
    devices = mesh.devices.reshape(mesh.shape["expert"], shard_size // quarters, quarters)
    split_mesh = Mesh(devices, ("expert", "zh", "y"))
    sh = ("zh", "y")
    return jax.shard_map(
        shards,
        mesh=split_mesh,
        in_specs=(
            P("expert", None),
            P("expert", None),
            P("expert", None),
            P(),
            P("expert", None, sh, None),
            P("expert", None, sh),
            P("expert", None, sh),
            P("expert", None, sh),
            P("expert", None, sh),
        ),
        out_specs=(
            P("expert", sh),
            P("expert", None, sh),
            P("expert", None, sh),
            P("expert", None, sh),
        ),
        check_vma=False,
    )
```

```python
import jax
import jax.numpy as jnp
from jax import lax
from jax.sharding import Mesh, PartitionSpec as P

STEP = 100


learn_rate = 0.01
beta_one = 0.9
beta_two = 0.999
epsilon = 1e-08
decay_rate = 0.1


def adamw(weight, gradient, first, second):
    grad_wide = gradient.astype(jnp.float32)
    first_new = beta_one * first + (1.0 - beta_one) * grad_wide
    second_new = beta_two * second + (1.0 - beta_two) * grad_wide * grad_wide
    first_hat = first_new / (1.0 - beta_one**STEP)
    second_hat = second_new / (1.0 - beta_two**STEP)
    weight_wide = weight.astype(jnp.float32)
    updated = weight_wide - learn_rate * (
        first_hat / (jnp.sqrt(second_hat) + epsilon) + decay_rate * weight_wide
    )
    return (updated.astype(jnp.bfloat16), first_new, second_new)


def shards(
    tokens,
    expert_ids,
    route_weights,
    partner,
    gate_up,
    down_weight,
    down_grad,
    moment_one,
    moment_two,
):
    groups = lax.axis_size("expert")
    quarters = lax.axis_size("y")
    token_count = tokens.shape[0]
    model_width = tokens.shape[1]
    part_width = down_weight.shape[2]
    trained = down_grad.shape[1]
    capacity = 2 * token_count * expert_ids.shape[1] // groups
    quarter = model_width // quarters
    new_rows, first_new, second_new = adamw(
        down_weight[:, :trained], down_grad, moment_one, moment_two
    )
    down_new = jnp.concatenate([new_rows, down_weight[:, trained:]], axis=1)
    pieces = (
        new_rows.reshape(groups, -1),
        first_new.astype(jnp.bfloat16).reshape(groups, -1),
        second_new.astype(jnp.bfloat16).reshape(groups, -1),
    )
    piece_width = sum(p.shape[1] for p in pieces)
    experts = jnp.arange(groups, dtype=jnp.int32)
    picked = (expert_ids[:, :, None] == experts[None, None, :]).astype(jnp.int32)
    running = jnp.cumsum(picked.reshape(-1, groups), axis=0).reshape(picked.shape)
    slot_index = jnp.sum((running - 1) * picked, axis=2)
    position = expert_ids * capacity + slot_index
    positions = jnp.arange(groups * capacity, dtype=jnp.int32)
    matches = position[None, :, :] == positions[:, None, None]
    dispatch = jnp.sum(matches.astype(jnp.int32), axis=2).astype(jnp.bfloat16)
    weighting = jnp.sum(jnp.where(matches, route_weights[None, :, :], 0.0), axis=2)
    own_quarter = lax.dynamic_slice_in_dim(tokens, lax.axis_index("y") * quarter, quarter, axis=1)
    outgoing = jnp.dot(dispatch, own_quarter, preferred_element_type=jnp.float32).astype(jnp.bfloat16)
    outgoing = jnp.concatenate([outgoing.reshape(groups, capacity * quarter)] + list(pieces), axis=1)
    joined = gate_up.reshape(-1, quarters, quarter)
    hidden_count = joined.shape[0] // 2
    every_weight = lax.all_gather(gate_up.reshape(-1, model_width), "y", axis=0, tiled=False)
    quarter_weights = lax.dynamic_slice_in_dim(every_weight, lax.axis_index("y") * quarter, quarter, axis=2)
    received = lax.all_to_all(outgoing, "expert", split_axis=0, concat_axis=0, tiled=True)
    spread = received[:, capacity * quarter :]
    received = received[:, : capacity * quarter].reshape(groups * capacity, quarter)
    partial = lax.dot_general(
        quarter_weights, received, (((2,), (1,)), ((), ())), preferred_element_type=jnp.float32
    )
    projected = lax.psum_scatter(partial, "y", scatter_dimension=0, tiled=False)
    hidden = (jax.nn.silu(projected[:hidden_count]) * projected[hidden_count:]).astype(jnp.bfloat16)
    back = lax.all_to_all(jnp.take(spread, partner, axis=0), "expert", split_axis=0, concat_axis=0, tiled=True)
    every_hidden = lax.all_gather(lax.all_gather(hidden, "y", axis=0, tiled=False), "zh", axis=0, tiled=False)
    every_hidden = every_hidden.reshape(-1, hidden.shape[1])
    down_rows = down_new.reshape(-1, part_width)
    summed = lax.dot_general(
        every_hidden, down_rows, (((0,), (0,)), ((), ())), preferred_element_type=jnp.float32
    )
    results = summed.astype(jnp.bfloat16).reshape(groups, capacity * part_width)
    returned = lax.all_to_all(results, "expert", split_axis=0, concat_axis=0, tiled=True)
    widths = [p.shape[1] for p in pieces]
    rows_out = back[:, : widths[0]].reshape(new_rows.shape)
    first_out = back[:, widths[0] : widths[0] + widths[1]].astype(jnp.float32).reshape(first_new.shape)
    second_out = back[:, widths[0] + widths[1] :].astype(jnp.float32).reshape(second_new.shape)
    returned_wide = returned.reshape(-1, part_width).astype(jnp.float32)
    combined = jnp.dot(
        weighting.T,
        returned_wide,
        precision=lax.Precision.HIGHEST,
        preferred_element_type=jnp.float32,
    ).astype(jnp.bfloat16)
    return (combined, rows_out, first_out, second_out)


def solution(mesh):
    shard_size = mesh.shape["shard"]
    quarters = 4 if shard_size % 4 == 0 else shard_size
    devices = mesh.devices.reshape(mesh.shape["expert"], shard_size // quarters, quarters)
    split_mesh = Mesh(devices, ("expert", "zh", "y"))
    sh = ("zh", "y")
    return jax.shard_map(
        shards,
        mesh=split_mesh,
        in_specs=(
            P("expert", None),
            P("expert", None),
            P("expert", None),
            P(),
            P("expert", None, sh, None),
            P("expert", None, sh),
            P("expert", None, sh),
            P("expert", None, sh),
            P("expert", None, sh),
        ),
        out_specs=(
            P("expert", sh),
            P("expert", None, sh),
            P("expert", None, sh),
            P("expert", None, sh),
        ),
        check_vma=False,
    )
```

```python
import jax
import jax.numpy as jnp
from jax import lax
from jax.sharding import Mesh, PartitionSpec as P

STEP = 100


learn_rate = 0.01
beta_one = 0.9
beta_two = 0.999
epsilon = 1e-08
decay_rate = 0.1


def adamw(weight, gradient, first, second):
    grad_wide = gradient.astype(jnp.float32)
    first_new = beta_one * first + (1.0 - beta_one) * grad_wide
    second_new = beta_two * second + (1.0 - beta_two) * grad_wide * grad_wide
    first_hat = first_new / (1.0 - beta_one**STEP)
    second_hat = second_new / (1.0 - beta_two**STEP)
    weight_wide = weight.astype(jnp.float32)
    updated = weight_wide - learn_rate * (
        first_hat / (jnp.sqrt(second_hat) + epsilon) + decay_rate * weight_wide
    )
    return (updated.astype(jnp.bfloat16), first_new, second_new)


def shards(
    tokens,
    expert_ids,
    route_weights,
    partner,
    gate_up,
    down_weight,
    down_grad,
    moment_one,
    moment_two,
):
    groups = lax.axis_size("expert")
    quarters = lax.axis_size("y")
    token_count = tokens.shape[0]
    model_width = tokens.shape[1]
    part_width = down_weight.shape[2]
    trained = down_grad.shape[1]
    capacity = 2 * token_count * expert_ids.shape[1] // groups
    quarter = model_width // quarters
    new_rows, first_new, second_new = adamw(
        down_weight[:, :trained], down_grad, moment_one, moment_two
    )
    down_new = jnp.concatenate([new_rows, down_weight[:, trained:]], axis=1)
    pieces = (
        new_rows.reshape(groups, -1),
        first_new.astype(jnp.bfloat16).reshape(groups, -1),
        second_new.astype(jnp.bfloat16).reshape(groups, -1),
    )
    piece_width = sum(p.shape[1] for p in pieces)
    experts = jnp.arange(groups, dtype=jnp.int32)
    picked = (expert_ids[:, :, None] == experts[None, None, :]).astype(jnp.int32)
    running = jnp.cumsum(picked.reshape(-1, groups), axis=0).reshape(picked.shape)
    slot_index = jnp.sum((running - 1) * picked, axis=2)
    position = expert_ids * capacity + slot_index
    positions = jnp.arange(groups * capacity, dtype=jnp.int32)
    matches = position[None, :, :] == positions[:, None, None]
    dispatch = jnp.sum(matches.astype(jnp.int32), axis=2).astype(jnp.bfloat16)
    weighting = jnp.sum(jnp.where(matches, route_weights[None, :, :], 0.0), axis=2)
    own_quarter = lax.dynamic_slice_in_dim(tokens, lax.axis_index("y") * quarter, quarter, axis=1)
    outgoing = jnp.dot(dispatch, own_quarter, preferred_element_type=jnp.float32).astype(jnp.bfloat16)
    outgoing = jnp.concatenate([outgoing.reshape(groups, capacity * quarter)] + list(pieces), axis=1)
    joined = gate_up.reshape(-1, quarters, quarter)
    hidden_count = joined.shape[0] // 2
    every_weight = lax.all_gather(gate_up.reshape(-1, model_width), "y", axis=0, tiled=False)
    quarter_weights = lax.dynamic_slice_in_dim(every_weight, lax.axis_index("y") * quarter, quarter, axis=2)
    received = lax.all_to_all(outgoing, "expert", split_axis=0, concat_axis=0, tiled=True)
    spread = received[:, capacity * quarter :]
    received = received[:, : capacity * quarter].reshape(groups * capacity, quarter)
    partial = lax.dot_general(
        quarter_weights, received, (((2,), (1,)), ((), ())), preferred_element_type=jnp.float32
    )
    projected = lax.psum_scatter(partial, "y", scatter_dimension=0, tiled=False)
    hidden = (jax.nn.silu(projected[:hidden_count]) * projected[hidden_count:]).astype(jnp.bfloat16)
    back = lax.all_to_all(jnp.take(spread, partner, axis=0), "expert", split_axis=0, concat_axis=0, tiled=True)
    every_hidden = lax.all_gather(lax.all_gather(hidden, "zh", axis=0, tiled=False), "y", axis=1, tiled=False)
    every_hidden = every_hidden.reshape(-1, hidden.shape[1])
    down_rows = down_new.reshape(-1, part_width)
    summed = lax.dot_general(
        every_hidden, down_rows, (((0,), (0,)), ((), ())), preferred_element_type=jnp.float32
    )
    results = summed.astype(jnp.bfloat16).reshape(groups, capacity * part_width)
    returned = lax.all_to_all(results, "expert", split_axis=0, concat_axis=0, tiled=True)
    widths = [p.shape[1] for p in pieces]
    rows_out = back[:, : widths[0]].reshape(new_rows.shape)
    first_out = back[:, widths[0] : widths[0] + widths[1]].astype(jnp.float32).reshape(first_new.shape)
    second_out = back[:, widths[0] + widths[1] :].astype(jnp.float32).reshape(second_new.shape)
    returned_wide = returned.reshape(-1, part_width).astype(jnp.float32)
    combined = jnp.dot(
        weighting.T,
        returned_wide,
        precision=lax.Precision.HIGHEST,
        preferred_element_type=jnp.float32,
    ).astype(jnp.bfloat16)
    return (combined, rows_out, first_out, second_out)


def solution(mesh):
    shard_size = mesh.shape["shard"]
    quarters = 4 if shard_size % 4 == 0 else shard_size
    devices = mesh.devices.reshape(mesh.shape["expert"], shard_size // quarters, quarters)
    split_mesh = Mesh(devices, ("expert", "zh", "y"))
    sh = ("zh", "y")
    return jax.shard_map(
        shards,
        mesh=split_mesh,
        in_specs=(
            P("expert", None),
            P("expert", None),
            P("expert", None),
            P(),
            P("expert", None, sh, None),
            P("expert", None, sh),
            P("expert", None, sh),
            P("expert", None, sh),
            P("expert", None, sh),
        ),
        out_specs=(
            P("expert", sh),
            P("expert", None, sh),
            P("expert", None, sh),
            P("expert", None, sh),
        ),
        check_vma=False,
    )
```

```python
import jax
import jax.numpy as jnp
from jax import lax
from jax.sharding import Mesh, PartitionSpec as P

STEP = 100


learn_rate = 0.01
beta_one = 0.9
beta_two = 0.999
epsilon = 1e-08
decay_rate = 0.1


def adamw(weight, gradient, first, second):
    grad_wide = gradient.astype(jnp.float32)
    first_new = beta_one * first + (1.0 - beta_one) * grad_wide
    second_new = beta_two * second + (1.0 - beta_two) * grad_wide * grad_wide
    first_hat = first_new / (1.0 - beta_one**STEP)
    second_hat = second_new / (1.0 - beta_two**STEP)
    weight_wide = weight.astype(jnp.float32)
    updated = weight_wide - learn_rate * (
        first_hat / (jnp.sqrt(second_hat) + epsilon) + decay_rate * weight_wide
    )
    return (updated.astype(jnp.bfloat16), first_new, second_new)


def shards(
    tokens,
    expert_ids,
    route_weights,
    partner,
    gate_up,
    down_weight,
    down_grad,
    moment_one,
    moment_two,
):
    groups = lax.axis_size("expert")
    quarters = lax.axis_size("y")
    token_count = tokens.shape[0]
    model_width = tokens.shape[1]
    part_width = down_weight.shape[2]
    trained = down_grad.shape[1]
    capacity = 2 * token_count * expert_ids.shape[1] // groups
    quarter = model_width // quarters
    new_rows, first_new, second_new = adamw(
        down_weight[:, :trained], down_grad, moment_one, moment_two
    )
    down_new = jnp.concatenate([new_rows, down_weight[:, trained:]], axis=1)
    pieces = (
        new_rows.reshape(groups, -1),
        first_new.astype(jnp.bfloat16).reshape(groups, -1),
        second_new.astype(jnp.bfloat16).reshape(groups, -1),
    )
    piece_width = sum(p.shape[1] for p in pieces)
    experts = jnp.arange(groups, dtype=jnp.int32)
    picked = (expert_ids[:, :, None] == experts[None, None, :]).astype(jnp.int32)
    running = jnp.cumsum(picked.reshape(-1, groups), axis=0).reshape(picked.shape)
    slot_index = jnp.sum((running - 1) * picked, axis=2)
    position = expert_ids * capacity + slot_index
    positions = jnp.arange(groups * capacity, dtype=jnp.int32)
    matches = position[None, :, :] == positions[:, None, None]
    dispatch = jnp.sum(matches.astype(jnp.int32), axis=2).astype(jnp.bfloat16)
    weighting = jnp.sum(jnp.where(matches, route_weights[None, :, :], 0.0), axis=2)
    own_quarter = lax.dynamic_slice_in_dim(tokens, lax.axis_index("y") * quarter, quarter, axis=1)
    outgoing = jnp.dot(dispatch, own_quarter, preferred_element_type=jnp.float32).astype(jnp.bfloat16)
    outgoing = outgoing.reshape(groups, capacity * quarter)
    joined = gate_up.reshape(-1, quarters, quarter)
    hidden_count = joined.shape[0] // 2
    every_weight = lax.all_gather(gate_up.reshape(-1, model_width), "y", axis=0, tiled=False)
    quarter_weights = lax.dynamic_slice_in_dim(every_weight, lax.axis_index("y") * quarter, quarter, axis=2)
    received = lax.all_to_all(outgoing, "expert", split_axis=0, concat_axis=0, tiled=True)
    received = received.reshape(groups * capacity, quarter)
    spread = lax.all_to_all(jnp.concatenate(pieces, axis=1), "expert", split_axis=0, concat_axis=0, tiled=True)
    partial = lax.dot_general(
        quarter_weights, received, (((2,), (1,)), ((), ())), preferred_element_type=jnp.float32
    )
    projected = lax.psum_scatter(partial, "y", scatter_dimension=0, tiled=False)
    hidden = (jax.nn.silu(projected[:hidden_count]) * projected[hidden_count:]).astype(jnp.bfloat16)
    back = lax.all_to_all(jnp.take(spread, partner, axis=0), "expert", split_axis=0, concat_axis=0, tiled=True)
    every_hidden = lax.all_gather(lax.all_gather(hidden, "zh", axis=0, tiled=False), "y", axis=1, tiled=False)
    every_hidden = every_hidden.reshape(-1, hidden.shape[1])
    down_rows = down_new.reshape(-1, part_width)
    summed = lax.dot_general(
        every_hidden, down_rows, (((0,), (0,)), ((), ())), preferred_element_type=jnp.float32
    )
    results = summed.astype(jnp.bfloat16).reshape(groups, capacity * part_width)
    returned = lax.all_to_all(results, "expert", split_axis=0, concat_axis=0, tiled=True)
    widths = [p.shape[1] for p in pieces]
    rows_out = back[:, : widths[0]].reshape(new_rows.shape)
    first_out = back[:, widths[0] : widths[0] + widths[1]].astype(jnp.float32).reshape(first_new.shape)
    second_out = back[:, widths[0] + widths[1] :].astype(jnp.float32).reshape(second_new.shape)
    returned_wide = returned.reshape(-1, part_width).astype(jnp.float32)
    combined = jnp.dot(
        weighting.T,
        returned_wide,
        precision=lax.Precision.HIGHEST,
        preferred_element_type=jnp.float32,
    ).astype(jnp.bfloat16)
    return (combined, rows_out, first_out, second_out)


def solution(mesh):
    shard_size = mesh.shape["shard"]
    quarters = 4 if shard_size % 4 == 0 else shard_size
    devices = mesh.devices.reshape(mesh.shape["expert"], shard_size // quarters, quarters)
    split_mesh = Mesh(devices, ("expert", "zh", "y"))
    sh = ("zh", "y")
    return jax.shard_map(
        shards,
        mesh=split_mesh,
        in_specs=(
            P("expert", None),
            P("expert", None),
            P("expert", None),
            P(),
            P("expert", None, sh, None),
            P("expert", None, sh),
            P("expert", None, sh),
            P("expert", None, sh),
            P("expert", None, sh),
        ),
        out_specs=(
            P("expert", sh),
            P("expert", None, sh),
            P("expert", None, sh),
            P("expert", None, sh),
        ),
        check_vma=False,
    )
```
